32 devices in a mesh: tile: 8 (over y, x, core), slab: 4 (over z).
Axes of the slice: x: 2, y: 2, z: 4, core: 2. Of those that a mesh axis runs over, the one named last changes fastest.
Arguments:
- estimate: float32 [64, 128, 512], P('slab', 'tile'), may hold values from 0.5 to 2
- observed: float32 [64, 128, 512], P('slab', 'tile'), may hold values from 0.25 to 4
- kernel_rows: float32 [31], replicated, may hold values from 0.001 to 1
- kernel_columns: float32 [31], replicated, may hold values from 0.001 to 1
- kernel_planes: float32 [31], replicated, may hold values from 0.001 to 1
Outputs:
- new_estimate: float32 [64, 128, 512], P('slab', 'tile')
- pyramid_level: float32 [64, 64, 256], P('slab', 'tile')
The draws below stay inside these ranges and needn't reach their ends.
All inputs are finite; a program needn't handle non-finite values.
Results may differ from the reference program's by a relative error of at most 0.00005.
Values sent between devices are 32-bit elements; how exact they have to be, the bound alone decides.
No kernel may reach another device: no remote copies, remote signals or barrier semaphores. Data moves between devices by JAX's collectives and lax.ppermute only.
A program may use at most 64 MiB of HBM per device.

```python
import math
import jax
import jax.numpy as jnp
from jax import lax

Y = 512
TAPS = 31
X = 128
Z = 64


def steps_of(key, dims, pieces, low, top_value):
    loudness = 1.0
    for dim, shards_of in pieces:
        draws = jax.random.uniform(jax.random.fold_in(jax.random.fold_in(key, 6), dim), (shards_of,), jnp.float32, low / len(pieces), top_value / len(pieces))
        loudness = loudness * jnp.repeat(jnp.exp(draws), dims[dim] // shards_of).reshape((-1,) + (1,) * (len(dims) - 1 - dim))
    return loudness


def setup_inputs(seed: int = 0) -> dict:
    key_list = jax.random.split(jax.random.key(seed), 6)
    estimate = jnp.clip(jnp.exp(math.log(2.0) - 1.3862944 * jax.random.uniform(key_list[0], (Z, X, Y), jnp.float32) ** steps_of(key_list[0], (Z, X, Y), ((0, 4), (1, 8)), -0.2, 0.2)), 0.5, 2.0)
    observed = jnp.clip(jnp.exp(math.log(4.0) - 2.7725887 * jax.random.uniform(key_list[1], (Z, X, Y), jnp.float32) ** steps_of(key_list[1], (Z, X, Y), ((0, 4), (1, 8)), -0.2, 0.2)), 0.25, 4.0)
    kernel_rows = jnp.clip(jnp.exp(jax.random.uniform(key_list[2], (TAPS,), jnp.float32, math.log(0.001), math.log(1.0))), 0.001, 1.0)
    kernel_columns = jnp.clip(jnp.exp(jax.random.uniform(key_list[3], (TAPS,), jnp.float32, math.log(0.001), math.log(1.0))), 0.001, 1.0)
    kernel_planes = jnp.clip(jnp.exp(jax.random.uniform(key_list[4], (TAPS,), jnp.float32, math.log(0.001), math.log(1.0))), 0.001, 1.0)
    return dict(estimate=estimate, observed=observed, kernel_rows=kernel_rows, kernel_columns=kernel_columns, kernel_planes=kernel_planes)


PRECISE = lax.Precision.HIGHEST


def banded(kernel, row_count, col_count, orient, anchor):
    tap_count = kernel.shape[0]
    offset_index = orient * (lax.broadcasted_iota(jnp.int32, (row_count, col_count), 0) - lax.broadcasted_iota(jnp.int32, (row_count, col_count), 1)) + anchor
    inside = (offset_index >= 0) & (offset_index < tap_count)
    values = jnp.take(kernel, jnp.clip(offset_index, 0, tap_count - 1))
    return jnp.where(inside, values, jnp.zeros_like(values))


def pyramid_matrix(row_count, col_count, anchor):
    offset_index = lax.broadcasted_iota(jnp.int32, (row_count, col_count), 0) - 2 * lax.broadcasted_iota(jnp.int32, (row_count, col_count), 1) + anchor
    outer = (offset_index == 0) | (offset_index == 3)
    middle = (offset_index == 1) | (offset_index == 2)
    return jnp.where(outer, jnp.float32(0.125), jnp.where(middle, jnp.float32(0.375), jnp.float32(0.0)))


def across_depth(volume, matrix):
    return jnp.einsum("pxy,pq->qxy", volume, matrix, precision=PRECISE)


def across_rows(volume, matrix):
    return jnp.einsum("zpy,pq->zqy", volume, matrix, precision=PRECISE)


def across_columns(volume, matrix):
    return jnp.einsum("zxp,pq->zxq", volume, matrix, precision=PRECISE)


def reference(estimate, observed, kernel_rows, kernel_columns, kernel_planes):
    plane_count, row_count, col_count = estimate.shape
    reach_cells = (kernel_rows.shape[0] - 1) // 2
    blurred = across_rows(estimate, banded(kernel_rows, row_count, row_count, 1, reach_cells))
    blurred = across_columns(blurred, banded(kernel_columns, col_count, col_count, 1, reach_cells))
    blurred = across_depth(blurred, banded(kernel_planes, plane_count, plane_count, 1, reach_cells))
    quotient = observed / blurred
    correction = across_depth(quotient, banded(kernel_planes, plane_count, plane_count, -1, reach_cells))
    correction = across_columns(correction, banded(kernel_columns, col_count, col_count, -1, reach_cells))
    correction = across_rows(correction, banded(kernel_rows, row_count, row_count, -1, reach_cells))
    new_estimate = estimate * correction
    halved = across_columns(new_estimate, pyramid_matrix(col_count, col_count // 2, 1))
    pyramid_level = across_rows(halved, pyramid_matrix(row_count, row_count // 2, 1))
    return new_estimate, pyramid_level
```

```python
import jax
import jax.numpy as jnp
from jax import lax
from jax.sharding import PartitionSpec as P

PRECISE = lax.Precision.HIGHEST


def halo(shard, axis, dim, before_width, after_width):
    devices, length = lax.axis_size(axis), shard.shape[dim]
    pieces_before, pieces_after = [], []
    hop = 1
    while (hop - 1) * length < max(before_width, after_width):
        up = [(i, i + hop) for i in range(devices - hop)]
        down = [(i + hop, i) for i in range(devices - hop)]
        if (hop - 1) * length < before_width:
            start = max(0, hop * length - before_width)
            piece = lax.slice_in_dim(shard, start, length, axis=dim)
            pieces_before.insert(0, lax.ppermute(piece, axis, up))
        if (hop - 1) * length < after_width:
            stop = min(length, after_width - (hop - 1) * length)
            piece = lax.slice_in_dim(shard, 0, stop, axis=dim)
            pieces_after.append(lax.ppermute(piece, axis, down))
        hop += 1
    return jnp.concatenate(pieces_before + [shard] + pieces_after, axis=dim)


def band(kernel, n_in, n_out, sign, shift):
    offset = sign * (
        lax.broadcasted_iota(jnp.int32, (n_in, n_out), 0)
        - lax.broadcasted_iota(jnp.int32, (n_in, n_out), 1)
    ) + shift
    matrix = jnp.zeros((n_in, n_out), jnp.float32)
    for tap in range(kernel.shape[0]):
        matrix = jnp.where(offset == tap, kernel[tap], matrix)
    return matrix


def band_square(kernel, n, shift):
    block = 128
    taps = kernel.shape[0]
    if n % block or n == block or max(shift, taps - 1 - shift) >= block:
        return band(kernel, n, n, 1, shift)
    count = n // block
    parts = {
        d: band(kernel, block, block, 1, shift + d * block) for d in (-1, 0, 1)
    }
    zero = jnp.zeros((block, block), jnp.float32)
    rows = [
        jnp.concatenate([parts.get(i - j, zero) for j in range(count)], axis=1)
        for i in range(count)
    ]
    return jnp.concatenate(rows, axis=0)


def pyramid_matrix(row_count, col_count, anchor):
    offset_index = (
        lax.broadcasted_iota(jnp.int32, (row_count, col_count), 0)
        - 2 * lax.broadcasted_iota(jnp.int32, (row_count, col_count), 1)
        + anchor
    )
    outer = (offset_index == 0) | (offset_index == 3)
    middle = (offset_index == 1) | (offset_index == 2)
    return jnp.where(
        outer, jnp.float32(0.125), jnp.where(middle, jnp.float32(0.375), jnp.float32(0.0))
    )


def along_columns(volume, matrix, transpose=False):
    contract = 1 if transpose else 0
    return lax.dot_general(
        volume, matrix, (((2,), (contract,)), ((), ())), precision=PRECISE
    )


def along_rows(volume, matrix):
    planes = volume.shape[0]
    left = jnp.broadcast_to(matrix.T[None], (planes,) + matrix.T.shape)
    return lax.dot_general(
        left, volume, (((2,), (1,)), ((0,), (0,))), precision=PRECISE
    )


def along_planes(volume, matrix):
    return lax.dot_general(
        matrix.T, volume, (((1,), (0,)), ((), ())), precision=PRECISE
    )


def shards(estimate, observed, kernel_rows, kernel_columns, kernel_planes):
    plane_count, row_count, col_count = estimate.shape
    taps = kernel_rows.shape[0]
    reach = (taps - 1) // 2

    estimate_ext = halo(estimate, "tile", 1, reach, reach)
    col_band = band_square(kernel_columns, col_count, reach)
    blurred = along_columns(estimate_ext, col_band)
    rows_ext = row_count + 2 * reach
    blurred = along_rows(blurred, band(kernel_rows, rows_ext, row_count, 1, 0))
    blurred = halo(blurred, "slab", 0, reach, reach)
    planes_ext = plane_count + 2 * reach
    blurred = along_planes(blurred, band(kernel_planes, planes_ext, plane_count, 1, 0))

    quotient = observed / blurred

    spread = halo(quotient, "slab", 0, reach, reach)
    spread = along_planes(
        spread, band(kernel_planes, planes_ext, plane_count, -1, 2 * reach)
    )
    spread = along_columns(spread, col_band, transpose=True)
    spread = halo(spread, "tile", 1, reach, reach)
    correction = along_rows(spread, band(kernel_rows, rows_ext, row_count, -1, 2 * reach))
    new_estimate = estimate * correction

    halved = along_columns(new_estimate, pyramid_matrix(col_count, col_count // 2, 1))
    halved = halo(halved, "tile", 1, 1, 1)
    pyramid_level = along_rows(halved, pyramid_matrix(row_count + 2, row_count // 2, 0))
    return (new_estimate, pyramid_level)


def solution(mesh):
    in_specs = (P("slab", "tile", None), P("slab", "tile", None), P(), P(), P())
    out_specs = (P("slab", "tile", None), P("slab", "tile", None))
    return jax.shard_map(shards, mesh=mesh, in_specs=in_specs, out_specs=out_specs, check_vma=False)
```

```python
import jax
import jax.numpy as jnp
from jax import lax
from jax.sharding import PartitionSpec as P

PRECISE = lax.Precision.HIGHEST


def halo(shard, axis, dim, before_width, after_width):
    devices, length = lax.axis_size(axis), shard.shape[dim]
    pieces_before, pieces_after = [], []
    hop = 1
    while (hop - 1) * length < max(before_width, after_width):
        up = [(i, i + hop) for i in range(devices - hop)]
        down = [(i + hop, i) for i in range(devices - hop)]
        if (hop - 1) * length < before_width:
            start = max(0, hop * length - before_width)
            piece = lax.slice_in_dim(shard, start, length, axis=dim)
            pieces_before.insert(0, lax.ppermute(piece, axis, up))
        if (hop - 1) * length < after_width:
            stop = min(length, after_width - (hop - 1) * length)
            piece = lax.slice_in_dim(shard, 0, stop, axis=dim)
            pieces_after.append(lax.ppermute(piece, axis, down))
        hop += 1
    return jnp.concatenate(pieces_before + [shard] + pieces_after, axis=dim)


def band(kernel, n_in, n_out, sign, shift):
    offset = sign * (
        lax.broadcasted_iota(jnp.int32, (n_in, n_out), 0)
        - lax.broadcasted_iota(jnp.int32, (n_in, n_out), 1)
    ) + shift
    taps = lax.broadcasted_iota(jnp.int32, (1, 1, kernel.shape[0]), 2)
    picked = jnp.where(offset[:, :, None] == taps, kernel[None, None, :], 0.0)
    return jnp.sum(picked, axis=2)


def band_square(kernel, n, shift):
    block = 128
    taps = kernel.shape[0]
    if n % block or n == block or max(shift, taps - 1 - shift) >= block:
        return band(kernel, n, n, 1, shift)
    count = n // block
    parts = {
        d: band(kernel, block, block, 1, shift + d * block) for d in (-1, 0, 1)
    }
    zero = jnp.zeros((block, block), jnp.float32)
    rows = [
        jnp.concatenate([parts.get(i - j, zero) for j in range(count)], axis=1)
        for i in range(count)
    ]
    return jnp.concatenate(rows, axis=0)


def pyramid_matrix(row_count, col_count, anchor):
    offset_index = (
        lax.broadcasted_iota(jnp.int32, (row_count, col_count), 0)
        - 2 * lax.broadcasted_iota(jnp.int32, (row_count, col_count), 1)
        + anchor
    )
    outer = (offset_index == 0) | (offset_index == 3)
    middle = (offset_index == 1) | (offset_index == 2)
    return jnp.where(
        outer, jnp.float32(0.125), jnp.where(middle, jnp.float32(0.375), jnp.float32(0.0))
    )


def along_columns(volume, matrix, transpose=False):
    contract = 1 if transpose else 0
    return lax.dot_general(
        volume, matrix, (((2,), (contract,)), ((), ())), precision=PRECISE
    )


def along_rows(volume, matrix):
    planes = volume.shape[0]
    left = jnp.broadcast_to(matrix.T[None], (planes,) + matrix.T.shape)
    return lax.dot_general(
        left, volume, (((2,), (1,)), ((0,), (0,))), precision=PRECISE
    )


def along_planes(volume, matrix):
    return lax.dot_general(
        matrix.T, volume, (((1,), (0,)), ((), ())), precision=PRECISE
    )


def shards(estimate, observed, kernel_rows, kernel_columns, kernel_planes):
    plane_count, row_count, col_count = estimate.shape
    taps = kernel_rows.shape[0]
    reach = (taps - 1) // 2

    rows_ext = row_count + 2 * reach
    planes_ext = plane_count + 2 * reach
    bands = lax.optimization_barrier((
        band_square(kernel_columns, col_count, reach),
        band(kernel_rows, rows_ext, row_count, 1, 0),
        band(kernel_planes, planes_ext, plane_count, 1, 0),
        band(kernel_planes, planes_ext, plane_count, -1, 2 * reach),
        band(kernel_rows, rows_ext, row_count, -1, 2 * reach),
        pyramid_matrix(col_count, col_count // 2, 1),
        pyramid_matrix(row_count + 2, row_count // 2, 0),
    ))
    col_band, row_fwd, plane_fwd, plane_back, row_back, pyr_cols, pyr_rows = bands

    estimate_ext = halo(estimate, "tile", 1, reach, reach)
    blurred = along_columns(estimate_ext, col_band)
    blurred = along_rows(blurred, row_fwd)
    blurred = halo(blurred, "slab", 0, reach, reach)
    blurred = along_planes(blurred, plane_fwd)

    quotient = observed / blurred

    spread = halo(quotient, "slab", 0, reach, reach)
    spread = along_planes(spread, plane_back)
    spread = along_columns(spread, col_band, transpose=True)
    spread = halo(spread, "tile", 1, reach, reach)
    correction = along_rows(spread, row_back)
    new_estimate = estimate * correction

    halved = along_columns(new_estimate, pyr_cols)
    halved = halo(halved, "tile", 1, 1, 1)
    pyramid_level = along_rows(halved, pyr_rows)
    return (new_estimate, pyramid_level)


def solution(mesh):
    in_specs = (P("slab", "tile", None), P("slab", "tile", None), P(), P(), P())
    out_specs = (P("slab", "tile", None), P("slab", "tile", None))
    return jax.shard_map(shards, mesh=mesh, in_specs=in_specs, out_specs=out_specs, check_vma=False)
```

```python
import jax
import jax.numpy as jnp
from jax import lax
from jax.sharding import PartitionSpec as P

PRECISE = lax.Precision.HIGHEST


def halo(shard, axis, dim, before_width, after_width):
    devices, length = lax.axis_size(axis), shard.shape[dim]
    pieces_before, pieces_after = [], []
    hop = 1
    while (hop - 1) * length < max(before_width, after_width):
        up = [(i, i + hop) for i in range(devices - hop)]
        down = [(i + hop, i) for i in range(devices - hop)]
        if (hop - 1) * length < before_width:
            start = max(0, hop * length - before_width)
            piece = lax.slice_in_dim(shard, start, length, axis=dim)
            pieces_before.insert(0, lax.ppermute(piece, axis, up))
        if (hop - 1) * length < after_width:
            stop = min(length, after_width - (hop - 1) * length)
            piece = lax.slice_in_dim(shard, 0, stop, axis=dim)
            pieces_after.append(lax.ppermute(piece, axis, down))
        hop += 1
    return jnp.concatenate(pieces_before + [shard] + pieces_after, axis=dim)


def band(kernel, n_in, n_out, sign, shift):
    offset = sign * (
        lax.broadcasted_iota(jnp.int32, (n_in, n_out), 0)
        - lax.broadcasted_iota(jnp.int32, (n_in, n_out), 1)
    ) + shift
    taps = lax.broadcasted_iota(jnp.int32, (1, 1, kernel.shape[0]), 2)
    picked = jnp.where(offset[:, :, None] == taps, kernel[None, None, :], 0.0)
    return jnp.sum(picked, axis=2)


def band_square(kernel, n, shift):
    block = 128
    taps = kernel.shape[0]
    if n % block or n == block or max(shift, taps - 1 - shift) >= block:
        return band(kernel, n, n, 1, shift)
    count = n // block
    parts = {
        d: band(kernel, block, block, 1, shift + d * block) for d in (-1, 0, 1)
    }
    zero = jnp.zeros((block, block), jnp.float32)
    rows = [
        jnp.concatenate([parts.get(i - j, zero) for j in range(count)], axis=1)
        for i in range(count)
    ]
    return jnp.concatenate(rows, axis=0)


def pyramid_matrix(row_count, col_count, anchor):
    offset_index = (
        lax.broadcasted_iota(jnp.int32, (row_count, col_count), 0)
        - 2 * lax.broadcasted_iota(jnp.int32, (row_count, col_count), 1)
        + anchor
    )
    outer = (offset_index == 0) | (offset_index == 3)
    middle = (offset_index == 1) | (offset_index == 2)
    return jnp.where(
        outer, jnp.float32(0.125), jnp.where(middle, jnp.float32(0.375), jnp.float32(0.0))
    )


def along_columns(volume, matrix, transpose=False):
    contract = 1 if transpose else 0
    return lax.dot_general(
        volume, matrix, (((2,), (contract,)), ((), ())), precision=PRECISE
    )


def along_rows(volume, matrix):
    planes = volume.shape[0]
    left = jnp.broadcast_to(matrix.T[None], (planes,) + matrix.T.shape)
    return lax.dot_general(
        left, volume, (((2,), (1,)), ((0,), (0,))), precision=PRECISE
    )


def along_planes(volume, matrix):
    return lax.dot_general(
        matrix.T, volume, (((1,), (0,)), ((), ())), precision=PRECISE
    )


def shards(estimate, observed, kernel_rows, kernel_columns, kernel_planes):
    plane_count, row_count, col_count = estimate.shape
    taps = kernel_rows.shape[0]
    reach = (taps - 1) // 2

    rows_ext = row_count + 2 * reach
    planes_ext = plane_count + 2 * reach
    bands = lax.optimization_barrier((
        band_square(kernel_columns, col_count, reach),
        band(kernel_rows, rows_ext, row_count, 1, 0),
        band(kernel_planes, planes_ext, plane_count, 1, 0),
        band(kernel_planes, planes_ext, plane_count, -1, 2 * reach),
        band(kernel_rows, rows_ext + 2, row_count + 2, -1, 2 * reach),
        pyramid_matrix(col_count, col_count // 2, 1),
        pyramid_matrix(row_count + 2, row_count // 2, 0),
    ))
    col_band, row_fwd, plane_fwd, plane_back, row_back, pyr_cols, pyr_rows = bands

    estimate_ext = halo(estimate, "tile", 1, reach, reach)
    blurred = along_columns(estimate_ext, col_band)
    blurred = along_rows(blurred, row_fwd)
    blurred = halo(blurred, "slab", 0, reach, reach)
    blurred = along_planes(blurred, plane_fwd)

    quotient = observed / blurred

    spread = halo(quotient, "slab", 0, reach, reach)
    spread = along_planes(spread, plane_back)
    spread = along_columns(spread, col_band, transpose=True)
    spread = halo(spread, "tile", 1, reach + 1, reach + 1)
    correction = along_rows(spread, row_back)
    edge_rows = lax.slice_in_dim(estimate_ext, reach - 1, reach + row_count + 1, axis=1)
    new_ext = edge_rows * correction
    new_estimate = lax.slice_in_dim(new_ext, 1, row_count + 1, axis=1)

    halved = along_columns(new_ext, pyr_cols)
    pyramid_level = along_rows(halved, pyr_rows)
    return (new_estimate, pyramid_level)


def solution(mesh):
    in_specs = (P("slab", "tile", None), P("slab", "tile", None), P(), P(), P())
    out_specs = (P("slab", "tile", None), P("slab", "tile", None))
    return jax.shard_map(shards, mesh=mesh, in_specs=in_specs, out_specs=out_specs, check_vma=False)
```

```python
import jax
import jax.numpy as jnp
from jax import lax
from jax.sharding import PartitionSpec as P

PRECISE = lax.Precision.HIGHEST
CHUNKS = 2


def halo(shard, axis, dim, before_width, after_width):
    devices, length = lax.axis_size(axis), shard.shape[dim]
    pieces_before, pieces_after = [], []
    hop = 1
    while (hop - 1) * length < max(before_width, after_width):
        up = [(i, i + hop) for i in range(devices - hop)]
        down = [(i + hop, i) for i in range(devices - hop)]
        if (hop - 1) * length < before_width:
            start = max(0, hop * length - before_width)
            piece = lax.slice_in_dim(shard, start, length, axis=dim)
            pieces_before.insert(0, lax.ppermute(piece, axis, up))
        if (hop - 1) * length < after_width:
            stop = min(length, after_width - (hop - 1) * length)
            piece = lax.slice_in_dim(shard, 0, stop, axis=dim)
            pieces_after.append(lax.ppermute(piece, axis, down))
        hop += 1
    return jnp.concatenate(pieces_before + [shard] + pieces_after, axis=dim)


def band(kernel, n_in, n_out, sign, shift):
    offset = sign * (
        lax.broadcasted_iota(jnp.int32, (n_in, n_out), 0)
        - lax.broadcasted_iota(jnp.int32, (n_in, n_out), 1)
    ) + shift
    taps = lax.broadcasted_iota(jnp.int32, (1, 1, kernel.shape[0]), 2)
    picked = jnp.where(offset[:, :, None] == taps, kernel[None, None, :], 0.0)
    return jnp.sum(picked, axis=2)


def band_square(kernel, n, shift):
    block = 128
    taps = kernel.shape[0]
    if n % block or n == block or max(shift, taps - 1 - shift) >= block:
        return band(kernel, n, n, 1, shift)
    count = n // block
    parts = {
        d: band(kernel, block, block, 1, shift + d * block) for d in (-1, 0, 1)
    }
    zero = jnp.zeros((block, block), jnp.float32)
    rows = [
        jnp.concatenate([parts.get(i - j, zero) for j in range(count)], axis=1)
        for i in range(count)
    ]
    return jnp.concatenate(rows, axis=0)


def pyramid_matrix(row_count, col_count, anchor):
    offset_index = (
        lax.broadcasted_iota(jnp.int32, (row_count, col_count), 0)
        - 2 * lax.broadcasted_iota(jnp.int32, (row_count, col_count), 1)
        + anchor
    )
    outer = (offset_index == 0) | (offset_index == 3)
    middle = (offset_index == 1) | (offset_index == 2)
    return jnp.where(
        outer, jnp.float32(0.125), jnp.where(middle, jnp.float32(0.375), jnp.float32(0.0))
    )


def along_columns(volume, matrix, transpose=False):
    contract = 1 if transpose else 0
    return lax.dot_general(
        volume, matrix, (((2,), (contract,)), ((), ())), precision=PRECISE
    )


def along_rows(volume, matrix):
    planes = volume.shape[0]
    left = jnp.broadcast_to(matrix.T[None], (planes,) + matrix.T.shape)
    return lax.dot_general(
        left, volume, (((2,), (1,)), ((0,), (0,))), precision=PRECISE
    )


def along_planes(volume, matrix):
    return lax.dot_general(
        matrix.T, volume, (((1,), (0,)), ((), ())), precision=PRECISE
    )


def shards(estimate, observed, kernel_rows, kernel_columns, kernel_planes):
    plane_count, row_count, col_count = estimate.shape
    taps = kernel_rows.shape[0]
    reach = (taps - 1) // 2

    rows_ext = row_count + 2 * reach
    planes_ext = plane_count + 2 * reach
    bands = lax.optimization_barrier((
        band_square(kernel_columns, col_count, reach),
        band(kernel_rows, rows_ext, row_count, 1, 0),
        band(kernel_planes, planes_ext, plane_count, 1, 0),
        band(kernel_planes, planes_ext, plane_count, -1, 2 * reach),
        band(kernel_rows, rows_ext + 2, row_count + 2, -1, 2 * reach),
        pyramid_matrix(col_count, col_count // 2, 1),
        pyramid_matrix(row_count + 2, row_count // 2, 0),
    ))
    col_band, row_fwd, plane_fwd, plane_back, row_back, pyr_cols, pyr_rows = bands

    filtered = along_columns(estimate, col_band)
    chunk = col_count // CHUNKS
    spreads = []
    for index in range(CHUNKS):
        part = lax.slice_in_dim(filtered, index * chunk, (index + 1) * chunk, axis=2)
        seen = lax.slice_in_dim(observed, index * chunk, (index + 1) * chunk, axis=2)
        blurred = along_planes(halo(part, "slab", 0, reach, reach), plane_fwd)
        blurred = along_rows(halo(blurred, "tile", 1, reach, reach), row_fwd)
        quotient = seen / blurred
        spread = along_planes(halo(quotient, "slab", 0, reach, reach), plane_back)
        spread = along_rows(halo(spread, "tile", 1, reach + 1, reach + 1), row_back)
        spreads.append(spread)
    correction = along_columns(jnp.concatenate(spreads, axis=2), col_band, transpose=True)
    edge_rows = halo(estimate, "tile", 1, 1, 1)
    new_ext = edge_rows * correction
    new_estimate = lax.slice_in_dim(new_ext, 1, row_count + 1, axis=1)

    halved = along_columns(new_ext, pyr_cols)
    pyramid_level = along_rows(halved, pyr_rows)
    return (new_estimate, pyramid_level)


def solution(mesh):
    in_specs = (P("slab", "tile", None), P("slab", "tile", None), P(), P(), P())
    out_specs = (P("slab", "tile", None), P("slab", "tile", None))
    return jax.shard_map(shards, mesh=mesh, in_specs=in_specs, out_specs=out_specs, check_vma=False)
```

```python
import jax
import jax.numpy as jnp
from jax import lax
from jax.sharding import PartitionSpec as P

PRECISE = lax.Precision.HIGHEST
CHUNKS = 2


def halo(shard, axis, dim, before_width, after_width, riders=None):
    devices, length = lax.axis_size(axis), shard.shape[dim]
    pieces_before, pieces_after = [], []
    carried = None
    hop = 1
    while (hop - 1) * length < max(before_width, after_width):
        up = [(i, i + hop) for i in range(devices - hop)]
        down = [(i + hop, i) for i in range(devices - hop)]
        start = max(0, hop * length - before_width)
        stop = min(length, after_width - (hop - 1) * length)
        send_up = lax.slice_in_dim(shard, start, length, axis=dim)
        send_down = lax.slice_in_dim(shard, 0, stop, axis=dim)
        if hop == 1 and riders is not None:
            send_up = jnp.concatenate([send_up, riders[0]], axis=dim)
            send_down = jnp.concatenate([send_down, riders[1]], axis=dim)
        got_up = lax.ppermute(send_up, axis, up)
        got_down = lax.ppermute(send_down, axis, down)
        if hop == 1 and riders is not None:
            width_up, width_down = length - start, stop
            carried = (
                lax.slice_in_dim(got_up, width_up, got_up.shape[dim], axis=dim),
                lax.slice_in_dim(got_down, width_down, got_down.shape[dim], axis=dim),
            )
            got_up = lax.slice_in_dim(got_up, 0, width_up, axis=dim)
            got_down = lax.slice_in_dim(got_down, 0, width_down, axis=dim)
        if (hop - 1) * length < before_width:
            pieces_before.insert(0, got_up)
        if (hop - 1) * length < after_width:
            pieces_after.append(got_down)
        hop += 1
    joined = jnp.concatenate(pieces_before + [shard] + pieces_after, axis=dim)
    return joined if riders is None else (joined, carried)


def band(kernel, n_in, n_out, sign, shift):
    offset = sign * (
        lax.broadcasted_iota(jnp.int32, (n_in, n_out), 0)
        - lax.broadcasted_iota(jnp.int32, (n_in, n_out), 1)
    ) + shift
    taps = lax.broadcasted_iota(jnp.int32, (1, 1, kernel.shape[0]), 2)
    picked = jnp.where(offset[:, :, None] == taps, kernel[None, None, :], 0.0)
    return jnp.sum(picked, axis=2)


def band_square(kernel, n, shift):
    block = 128
    taps = kernel.shape[0]
    if n % block or n == block or max(shift, taps - 1 - shift) >= block:
        return band(kernel, n, n, 1, shift)
    count = n // block
    parts = {
        d: band(kernel, block, block, 1, shift + d * block) for d in (-1, 0, 1)
    }
    zero = jnp.zeros((block, block), jnp.float32)
    rows = [
        jnp.concatenate([parts.get(i - j, zero) for j in range(count)], axis=1)
        for i in range(count)
    ]
    return jnp.concatenate(rows, axis=0)


def pyramid_matrix(row_count, col_count, anchor):
    offset_index = (
        lax.broadcasted_iota(jnp.int32, (row_count, col_count), 0)
        - 2 * lax.broadcasted_iota(jnp.int32, (row_count, col_count), 1)
        + anchor
    )
    outer = (offset_index == 0) | (offset_index == 3)
    middle = (offset_index == 1) | (offset_index == 2)
    return jnp.where(
        outer, jnp.float32(0.125), jnp.where(middle, jnp.float32(0.375), jnp.float32(0.0))
    )


def along_columns(volume, matrix, transpose=False):
    contract = 1 if transpose else 0
    return lax.dot_general(
        volume, matrix, (((2,), (contract,)), ((), ())), precision=PRECISE
    )


def along_rows(volume, matrix):
    planes = volume.shape[0]
    left = jnp.broadcast_to(matrix.T[None], (planes,) + matrix.T.shape)
    return lax.dot_general(
        left, volume, (((2,), (1,)), ((0,), (0,))), precision=PRECISE
    )


def along_planes(volume, matrix):
    return lax.dot_general(
        matrix.T, volume, (((1,), (0,)), ((), ())), precision=PRECISE
    )


def shards(estimate, observed, kernel_rows, kernel_columns, kernel_planes):
    plane_count, row_count, col_count = estimate.shape
    taps = kernel_rows.shape[0]
    reach = (taps - 1) // 2

    rows_ext = row_count + 2 * reach
    planes_ext = plane_count + 2 * reach
    bands = lax.optimization_barrier((
        band_square(kernel_columns, col_count, reach),
        band(kernel_rows, rows_ext, row_count, 1, 0),
        band(kernel_planes, planes_ext, plane_count, 1, 0),
        band(kernel_planes, planes_ext, plane_count, -1, 2 * reach),
        band(kernel_rows, rows_ext + 2, row_count + 2, -1, 2 * reach),
        pyramid_matrix(col_count, col_count // 2, 1),
        pyramid_matrix(row_count + 2, row_count // 2, 0),
    ))
    col_band, row_fwd, plane_fwd, plane_back, row_back, pyr_cols, pyr_rows = bands

    filtered = along_columns(estimate, col_band)
    chunk = col_count // CHUNKS
    planes = plane_count
    last_row = lax.slice_in_dim(estimate, row_count - 1, row_count, axis=1)
    first_row = lax.slice_in_dim(estimate, 0, 1, axis=1)
    fold = (planes, CHUNKS, chunk)
    riders = (last_row.reshape(fold), first_row.reshape(fold))
    spreads = []
    for index in range(CHUNKS):
        part = lax.slice_in_dim(filtered, index * chunk, (index + 1) * chunk, axis=2)
        seen = lax.slice_in_dim(observed, index * chunk, (index + 1) * chunk, axis=2)
        blurred = along_planes(halo(part, "slab", 0, reach, reach), plane_fwd)
        if index == 0:
            blurred, carried = halo(blurred, "tile", 1, reach, reach, riders)
        else:
            blurred = halo(blurred, "tile", 1, reach, reach)
        blurred = along_rows(blurred, row_fwd)
        quotient = seen / blurred
        spread = along_planes(halo(quotient, "slab", 0, reach, reach), plane_back)
        spread = along_rows(halo(spread, "tile", 1, reach + 1, reach + 1), row_back)
        spreads.append(spread)
    correction = along_columns(jnp.concatenate(spreads, axis=2), col_band, transpose=True)
    unfold = (planes, 1, col_count)
    edge_rows = jnp.concatenate(
        [carried[0].reshape(unfold), estimate, carried[1].reshape(unfold)], axis=1
    )
    new_ext = edge_rows * correction
    new_estimate = lax.slice_in_dim(new_ext, 1, row_count + 1, axis=1)

    halved = along_columns(new_ext, pyr_cols)
    pyramid_level = along_rows(halved, pyr_rows)
    return (new_estimate, pyramid_level)


def solution(mesh):
    in_specs = (P("slab", "tile", None), P("slab", "tile", None), P(), P(), P())
    out_specs = (P("slab", "tile", None), P("slab", "tile", None))
    return jax.shard_map(shards, mesh=mesh, in_specs=in_specs, out_specs=out_specs, check_vma=False)
```

```python
import jax
import jax.numpy as jnp
from jax import lax
from jax.sharding import PartitionSpec as P

PRECISE = lax.Precision.HIGH
CHUNKS = 2


def halo(shard, axis, dim, before_width, after_width, riders=None):
    devices, length = lax.axis_size(axis), shard.shape[dim]
    pieces_before, pieces_after = [], []
    carried = None
    hop = 1
    while (hop - 1) * length < max(before_width, after_width):
        up = [(i, i + hop) for i in range(devices - hop)]
        down = [(i + hop, i) for i in range(devices - hop)]
        start = max(0, hop * length - before_width)
        stop = min(length, after_width - (hop - 1) * length)
        send_up = lax.slice_in_dim(shard, start, length, axis=dim)
        send_down = lax.slice_in_dim(shard, 0, stop, axis=dim)
        if hop == 1 and riders is not None:
            send_up = jnp.concatenate([send_up, riders[0]], axis=dim)
            send_down = jnp.concatenate([send_down, riders[1]], axis=dim)
        got_up = lax.ppermute(send_up, axis, up)
        got_down = lax.ppermute(send_down, axis, down)
        if hop == 1 and riders is not None:
            width_up, width_down = length - start, stop
            carried = (
                lax.slice_in_dim(got_up, width_up, got_up.shape[dim], axis=dim),
                lax.slice_in_dim(got_down, width_down, got_down.shape[dim], axis=dim),
            )
            got_up = lax.slice_in_dim(got_up, 0, width_up, axis=dim)
            got_down = lax.slice_in_dim(got_down, 0, width_down, axis=dim)
        if (hop - 1) * length < before_width:
            pieces_before.insert(0, got_up)
        if (hop - 1) * length < after_width:
            pieces_after.append(got_down)
        hop += 1
    joined = jnp.concatenate(pieces_before + [shard] + pieces_after, axis=dim)
    return joined if riders is None else (joined, carried)


def band(kernel, n_in, n_out, sign, shift):
    offset = sign * (
        lax.broadcasted_iota(jnp.int32, (n_in, n_out), 0)
        - lax.broadcasted_iota(jnp.int32, (n_in, n_out), 1)
    ) + shift
    taps = lax.broadcasted_iota(jnp.int32, (1, 1, kernel.shape[0]), 2)
    picked = jnp.where(offset[:, :, None] == taps, kernel[None, None, :], 0.0)
    return jnp.sum(picked, axis=2)


def band_square(kernel, n, shift):
    block = 128
    taps = kernel.shape[0]
    if n % block or n == block or max(shift, taps - 1 - shift) >= block:
        return band(kernel, n, n, 1, shift)
    count = n // block
    parts = {
        d: band(kernel, block, block, 1, shift + d * block) for d in (-1, 0, 1)
    }
    zero = jnp.zeros((block, block), jnp.float32)
    rows = [
        jnp.concatenate([parts.get(i - j, zero) for j in range(count)], axis=1)
        for i in range(count)
    ]
    return jnp.concatenate(rows, axis=0)


def pyramid_matrix(row_count, col_count, anchor):
    offset_index = (
        lax.broadcasted_iota(jnp.int32, (row_count, col_count), 0)
        - 2 * lax.broadcasted_iota(jnp.int32, (row_count, col_count), 1)
        + anchor
    )
    outer = (offset_index == 0) | (offset_index == 3)
    middle = (offset_index == 1) | (offset_index == 2)
    return jnp.where(
        outer, jnp.float32(0.125), jnp.where(middle, jnp.float32(0.375), jnp.float32(0.0))
    )


def along_columns(volume, matrix, transpose=False):
    contract = 1 if transpose else 0
    return lax.dot_general(
        volume, matrix, (((2,), (contract,)), ((), ())), precision=PRECISE
    )


def along_rows(volume, matrix):
    planes = volume.shape[0]
    left = jnp.broadcast_to(matrix.T[None], (planes,) + matrix.T.shape)
    return lax.dot_general(
        left, volume, (((2,), (1,)), ((0,), (0,))), precision=PRECISE
    )


def along_planes(volume, matrix):
    return lax.dot_general(
        matrix.T, volume, (((1,), (0,)), ((), ())), precision=PRECISE
    )


def shards(estimate, observed, kernel_rows, kernel_columns, kernel_planes):
    plane_count, row_count, col_count = estimate.shape
    taps = kernel_rows.shape[0]
    reach = (taps - 1) // 2

    rows_ext = row_count + 2 * reach
    planes_ext = plane_count + 2 * reach
    bands = lax.optimization_barrier((
        band_square(kernel_columns, col_count, reach),
        band(kernel_rows, rows_ext, row_count, 1, 0),
        band(kernel_planes, planes_ext, plane_count, 1, 0),
        band(kernel_planes, planes_ext, plane_count, -1, 2 * reach),
        band(kernel_rows, rows_ext + 2, row_count + 2, -1, 2 * reach),
        pyramid_matrix(col_count, col_count // 2, 1),
        pyramid_matrix(row_count + 2, row_count // 2, 0),
    ))
    col_band, row_fwd, plane_fwd, plane_back, row_back, pyr_cols, pyr_rows = bands

    filtered = along_columns(estimate, col_band)
    chunk = col_count // CHUNKS
    planes = plane_count
    last_row = lax.slice_in_dim(estimate, row_count - 1, row_count, axis=1)
    first_row = lax.slice_in_dim(estimate, 0, 1, axis=1)
    fold = (planes, CHUNKS, chunk)
    riders = (last_row.reshape(fold), first_row.reshape(fold))
    spreads = []
    for index in range(CHUNKS):
        part = lax.slice_in_dim(filtered, index * chunk, (index + 1) * chunk, axis=2)
        seen = lax.slice_in_dim(observed, index * chunk, (index + 1) * chunk, axis=2)
        blurred = along_planes(halo(part, "slab", 0, reach, reach), plane_fwd)
        if index == 0:
            blurred, carried = halo(blurred, "tile", 1, reach, reach, riders)
        else:
            blurred = halo(blurred, "tile", 1, reach, reach)
        blurred = along_rows(blurred, row_fwd)
        quotient = seen / blurred
        spread = along_planes(halo(quotient, "slab", 0, reach, reach), plane_back)
        spread = along_rows(halo(spread, "tile", 1, reach + 1, reach + 1), row_back)
        spreads.append(spread)
    correction = along_columns(jnp.concatenate(spreads, axis=2), col_band, transpose=True)
    unfold = (planes, 1, col_count)
    edge_rows = jnp.concatenate(
        [carried[0].reshape(unfold), estimate, carried[1].reshape(unfold)], axis=1
    )
    new_ext = edge_rows * correction
    new_estimate = lax.slice_in_dim(new_ext, 1, row_count + 1, axis=1)

    halved = along_columns(new_ext, pyr_cols)
    pyramid_level = along_rows(halved, pyr_rows)
    return (new_estimate, pyramid_level)


def solution(mesh):
    in_specs = (P("slab", "tile", None), P("slab", "tile", None), P(), P(), P())
    out_specs = (P("slab", "tile", None), P("slab", "tile", None))
    return jax.shard_map(shards, mesh=mesh, in_specs=in_specs, out_specs=out_specs, check_vma=False)
```

```python
import jax
import jax.numpy as jnp
from jax import lax
from jax.sharding import PartitionSpec as P

PRECISE = lax.Precision.HIGH
CHUNKS = 2


def halo(shard, axis, dim, before_width, after_width, riders=None):
    devices, length = lax.axis_size(axis), shard.shape[dim]
    pieces_before, pieces_after = [], []
    carried = None
    hop = 1
    while (hop - 1) * length < max(before_width, after_width):
        up = [(i, i + hop) for i in range(devices - hop)]
        down = [(i + hop, i) for i in range(devices - hop)]
        start = max(0, hop * length - before_width)
        stop = min(length, after_width - (hop - 1) * length)
        send_up = lax.slice_in_dim(shard, start, length, axis=dim)
        send_down = lax.slice_in_dim(shard, 0, stop, axis=dim)
        if hop == 1 and riders is not None:
            send_up = jnp.concatenate([send_up, riders[0]], axis=dim)
            send_down = jnp.concatenate([send_down, riders[1]], axis=dim)
        got_up = lax.ppermute(send_up, axis, up)
        got_down = lax.ppermute(send_down, axis, down)
        if hop == 1 and riders is not None:
            width_up, width_down = length - start, stop
            carried = (
                lax.slice_in_dim(got_up, width_up, got_up.shape[dim], axis=dim),
                lax.slice_in_dim(got_down, width_down, got_down.shape[dim], axis=dim),
            )
            got_up = lax.slice_in_dim(got_up, 0, width_up, axis=dim)
            got_down = lax.slice_in_dim(got_down, 0, width_down, axis=dim)
        if (hop - 1) * length < before_width:
            pieces_before.insert(0, got_up)
        if (hop - 1) * length < after_width:
            pieces_after.append(got_down)
        hop += 1
    joined = jnp.concatenate(pieces_before + [shard] + pieces_after, axis=dim)
    return joined if riders is None else (joined, carried)


def band(kernel, n_in, n_out, sign, shift):
    offset = sign * (
        lax.broadcasted_iota(jnp.int32, (n_in, n_out), 0)
        - lax.broadcasted_iota(jnp.int32, (n_in, n_out), 1)
    ) + shift
    taps = lax.broadcasted_iota(jnp.int32, (1, 1, kernel.shape[0]), 2)
    picked = jnp.where(offset[:, :, None] == taps, kernel[None, None, :], 0.0)
    return jnp.sum(picked, axis=2)


def band_square(kernel, n, shift):
    block = 128
    taps = kernel.shape[0]
    if n % block or n == block or max(shift, taps - 1 - shift) >= block:
        return band(kernel, n, n, 1, shift)
    count = n // block
    parts = {
        d: band(kernel, block, block, 1, shift + d * block) for d in (-1, 0, 1)
    }
    zero = jnp.zeros((block, block), jnp.float32)
    rows = [
        jnp.concatenate([parts.get(i - j, zero) for j in range(count)], axis=1)
        for i in range(count)
    ]
    return jnp.concatenate(rows, axis=0)


def pyramid_matrix(row_count, col_count, anchor):
    offset_index = (
        lax.broadcasted_iota(jnp.int32, (row_count, col_count), 0)
        - 2 * lax.broadcasted_iota(jnp.int32, (row_count, col_count), 1)
        + anchor
    )
    outer = (offset_index == 0) | (offset_index == 3)
    middle = (offset_index == 1) | (offset_index == 2)
    return jnp.where(
        outer, jnp.float32(0.125), jnp.where(middle, jnp.float32(0.375), jnp.float32(0.0))
    )


def along_columns(volume, matrix, transpose=False):
    contract = 1 if transpose else 0
    return lax.dot_general(
        volume, matrix, (((2,), (contract,)), ((), ())), precision=PRECISE
    )


def along_rows(volume, matrix):
    planes = volume.shape[0]
    left = jnp.broadcast_to(matrix.T[None], (planes,) + matrix.T.shape)
    return lax.dot_general(
        left, volume, (((2,), (1,)), ((0,), (0,))), precision=PRECISE
    )


def along_planes(volume, matrix):
    return lax.dot_general(
        matrix.T, volume, (((1,), (0,)), ((), ())), precision=PRECISE
    )


def shards(estimate, observed, kernel_rows, kernel_columns, kernel_planes):
    plane_count, row_count, col_count = estimate.shape
    taps = kernel_rows.shape[0]
    reach = (taps - 1) // 2

    rows_ext = row_count + 2 * reach
    planes_ext = plane_count + 2 * reach
    bands = [
        band_square(kernel_columns, col_count, reach),
        band(kernel_rows, rows_ext, row_count, 1, 0),
        band(kernel_planes, planes_ext, plane_count, 1, 0),
        band(kernel_planes, planes_ext, plane_count, -1, 2 * reach),
        band(kernel_rows, rows_ext + 2, row_count + 2, -1, 2 * reach),
        pyramid_matrix(col_count, col_count // 2, 1),
        pyramid_matrix(row_count + 2, row_count // 2, 0),
    ]
    bands = [lax.optimization_barrier(matrix) for matrix in bands]
    col_band, row_fwd, plane_fwd, plane_back, row_back, pyr_cols, pyr_rows = bands

    filtered = along_columns(estimate, col_band)
    chunk = col_count // CHUNKS
    planes = plane_count
    last_row = lax.slice_in_dim(estimate, row_count - 1, row_count, axis=1)
    first_row = lax.slice_in_dim(estimate, 0, 1, axis=1)
    fold = (planes, CHUNKS, chunk)
    riders = (last_row.reshape(fold), first_row.reshape(fold))
    spreads = []
    for index in range(CHUNKS):
        part = lax.slice_in_dim(filtered, index * chunk, (index + 1) * chunk, axis=2)
        seen = lax.slice_in_dim(observed, index * chunk, (index + 1) * chunk, axis=2)
        blurred = along_planes(halo(part, "slab", 0, reach, reach), plane_fwd)
        if index == 0:
            blurred, carried = halo(blurred, "tile", 1, reach, reach, riders)
        else:
            blurred = halo(blurred, "tile", 1, reach, reach)
        blurred = along_rows(blurred, row_fwd)
        quotient = seen / blurred
        spread = along_planes(halo(quotient, "slab", 0, reach, reach), plane_back)
        spread = along_rows(halo(spread, "tile", 1, reach + 1, reach + 1), row_back)
        cols_of = lax.slice_in_dim(col_band, index * chunk, (index + 1) * chunk, axis=1)
        share = along_columns(spread, cols_of, transpose=True)
        spreads.append(share)
    correction = spreads[0]
    for share in spreads[1:]:
        correction = correction + share
    unfold = (planes, 1, col_count)
    edge_rows = jnp.concatenate(
        [carried[0].reshape(unfold), estimate, carried[1].reshape(unfold)], axis=1
    )
    new_ext = edge_rows * correction
    new_estimate = estimate * lax.slice_in_dim(correction, 1, row_count + 1, axis=1)

    halved = along_columns(new_ext, pyr_cols)
    pyramid_level = along_rows(halved, pyr_rows)
    return (new_estimate, pyramid_level)


def solution(mesh):
    in_specs = (P("slab", "tile", None), P("slab", "tile", None), P(), P(), P())
    out_specs = (P("slab", "tile", None), P("slab", "tile", None))
    return jax.shard_map(shards, mesh=mesh, in_specs=in_specs, out_specs=out_specs, check_vma=False)
```

```python
import jax
import jax.numpy as jnp
from jax import lax
from jax.sharding import PartitionSpec as P

PRECISE = lax.Precision.HIGH
CHUNKS = 2


def halo(shard, axis, dim, before_width, after_width, riders=None):
    devices, length = lax.axis_size(axis), shard.shape[dim]
    pieces_before, pieces_after = [], []
    carried = None
    hop = 1
    while (hop - 1) * length < max(before_width, after_width):
        up = [(i, i + hop) for i in range(devices - hop)]
        down = [(i + hop, i) for i in range(devices - hop)]
        start = max(0, hop * length - before_width)
        stop = min(length, after_width - (hop - 1) * length)
        send_up = lax.slice_in_dim(shard, start, length, axis=dim)
        send_down = lax.slice_in_dim(shard, 0, stop, axis=dim)
        if hop == 1 and riders is not None:
            send_up = jnp.concatenate([send_up, riders[0]], axis=dim)
            send_down = jnp.concatenate([send_down, riders[1]], axis=dim)
        got_up = lax.ppermute(send_up, axis, up)
        got_down = lax.ppermute(send_down, axis, down)
        if hop == 1 and riders is not None:
            width_up, width_down = length - start, stop
            carried = (
                lax.slice_in_dim(got_up, width_up, got_up.shape[dim], axis=dim),
                lax.slice_in_dim(got_down, width_down, got_down.shape[dim], axis=dim),
            )
            got_up = lax.slice_in_dim(got_up, 0, width_up, axis=dim)
            got_down = lax.slice_in_dim(got_down, 0, width_down, axis=dim)
        if (hop - 1) * length < before_width:
            pieces_before.insert(0, got_up)
        if (hop - 1) * length < after_width:
            pieces_after.append(got_down)
        hop += 1
    joined = jnp.concatenate(pieces_before + [shard] + pieces_after, axis=dim)
    return joined if riders is None else (joined, carried)


def band(kernel, n_in, n_out, sign, shift):
    offset = sign * (
        lax.broadcasted_iota(jnp.int32, (n_in, n_out), 0)
        - lax.broadcasted_iota(jnp.int32, (n_in, n_out), 1)
    ) + shift
    taps = lax.broadcasted_iota(jnp.int32, (1, 1, kernel.shape[0]), 2)
    picked = jnp.where(offset[:, :, None] == taps, kernel[None, None, :], 0.0)
    return jnp.sum(picked, axis=2)


def band_square(kernel, n, shift):
    block = 128
    taps = kernel.shape[0]
    if n % block or n == block or max(shift, taps - 1 - shift) >= block:
        return band(kernel, n, n, 1, shift)
    count = n // block
    parts = {
        d: band(kernel, block, block, 1, shift + d * block) for d in (-1, 0, 1)
    }
    zero = jnp.zeros((block, block), jnp.float32)
    rows = [
        jnp.concatenate([parts.get(i - j, zero) for j in range(count)], axis=1)
        for i in range(count)
    ]
    return jnp.concatenate(rows, axis=0)


def pyramid_matrix(row_count, col_count, anchor):
    offset_index = (
        lax.broadcasted_iota(jnp.int32, (row_count, col_count), 0)
        - 2 * lax.broadcasted_iota(jnp.int32, (row_count, col_count), 1)
        + anchor
    )
    outer = (offset_index == 0) | (offset_index == 3)
    middle = (offset_index == 1) | (offset_index == 2)
    return jnp.where(
        outer, jnp.float32(0.125), jnp.where(middle, jnp.float32(0.375), jnp.float32(0.0))
    )


def along_columns(volume, matrix, transpose=False):
    contract = 1 if transpose else 0
    return lax.dot_general(
        volume, matrix, (((2,), (contract,)), ((), ())), precision=PRECISE
    )


def along_rows(volume, matrix):
    planes = volume.shape[0]
    left = jnp.broadcast_to(matrix.T[None], (planes,) + matrix.T.shape)
    return lax.dot_general(
        left, volume, (((2,), (1,)), ((0,), (0,))), precision=PRECISE
    )


def along_planes(volume, matrix):
    return lax.dot_general(
        matrix.T, volume, (((1,), (0,)), ((), ())), precision=PRECISE
    )


def shards(estimate, observed, kernel_rows, kernel_columns, kernel_planes):
    plane_count, row_count, col_count = estimate.shape
    taps = kernel_rows.shape[0]
    reach = (taps - 1) // 2

    rows_ext = row_count + 2 * reach
    planes_ext = plane_count + 2 * reach
    bands = [
        band_square(kernel_columns, col_count, reach),
        band(kernel_rows, rows_ext, row_count, 1, 0),
        band(kernel_planes, planes_ext, plane_count, 1, 0),
        band(kernel_planes, planes_ext, plane_count, -1, 2 * reach),
        band(kernel_rows, rows_ext + 2, row_count + 2, -1, 2 * reach),
        pyramid_matrix(col_count, col_count // 2, 1),
        pyramid_matrix(row_count + 2, row_count // 2, 0),
    ]
    bands = [lax.optimization_barrier(matrix) for matrix in bands]
    col_band, row_fwd, plane_fwd, plane_back, row_back, pyr_cols, pyr_rows = bands

    filtered = along_columns(estimate, col_band)
    chunk = col_count // CHUNKS
    planes = plane_count
    last_row = lax.slice_in_dim(estimate, row_count - 1, row_count, axis=1)
    first_row = lax.slice_in_dim(estimate, 0, 1, axis=1)
    fold = (planes, CHUNKS, chunk)
    riders = (last_row.reshape(fold), first_row.reshape(fold))
    spreads = []
    for index in range(CHUNKS):
        part = lax.slice_in_dim(filtered, index * chunk, (index + 1) * chunk, axis=2)
        seen = lax.slice_in_dim(observed, index * chunk, (index + 1) * chunk, axis=2)
        z_first = index % 2 == 0
        blurred = part
        for along_z in ((True, False) if z_first else (False, True)):
            if along_z:
                blurred = along_planes(halo(blurred, "slab", 0, reach, reach), plane_fwd)
            elif index == 0:
                blurred, carried = halo(blurred, "tile", 1, reach, reach, riders)
                blurred = along_rows(blurred, row_fwd)
            else:
                blurred = along_rows(halo(blurred, "tile", 1, reach, reach), row_fwd)
        quotient = seen / blurred
        spread = quotient
        for along_z in ((True, False) if z_first else (False, True)):
            if along_z:
                spread = along_planes(halo(spread, "slab", 0, reach, reach), plane_back)
            else:
                spread = along_rows(halo(spread, "tile", 1, reach + 1, reach + 1), row_back)
        cols_of = lax.slice_in_dim(col_band, index * chunk, (index + 1) * chunk, axis=1)
        share = along_columns(spread, cols_of, transpose=True)
        spreads.append(share)
    correction = spreads[0]
    for share in spreads[1:]:
        correction = correction + share
    unfold = (planes, 1, col_count)
    edge_rows = jnp.concatenate(
        [carried[0].reshape(unfold), estimate, carried[1].reshape(unfold)], axis=1
    )
    new_ext = edge_rows * correction
    new_estimate = estimate * lax.slice_in_dim(correction, 1, row_count + 1, axis=1)

    halved = along_columns(new_ext, pyr_cols)
    pyramid_level = along_rows(halved, pyr_rows)
    return (new_estimate, pyramid_level)


def solution(mesh):
    in_specs = (P("slab", "tile", None), P("slab", "tile", None), P(), P(), P())
    out_specs = (P("slab", "tile", None), P("slab", "tile", None))
    return jax.shard_map(shards, mesh=mesh, in_specs=in_specs, out_specs=out_specs, check_vma=False)
```

```python
import jax
import jax.numpy as jnp
from jax import lax
from jax.sharding import PartitionSpec as P

PRECISE = lax.Precision.HIGH
CHUNKS = 2


def halo(shard, axis, dim, before_width, after_width, riders=None):
    devices, length = lax.axis_size(axis), shard.shape[dim]
    pieces_before, pieces_after = [], []
    carried = None
    hop = 1
    while (hop - 1) * length < max(before_width, after_width):
        up = [(i, i + hop) for i in range(devices - hop)]
        down = [(i + hop, i) for i in range(devices - hop)]
        start = max(0, hop * length - before_width)
        stop = min(length, after_width - (hop - 1) * length)
        send_up = lax.slice_in_dim(shard, start, length, axis=dim)
        send_down = lax.slice_in_dim(shard, 0, stop, axis=dim)
        if hop == 1 and riders is not None:
            send_up = jnp.concatenate([send_up, riders[0]], axis=dim)
            send_down = jnp.concatenate([send_down, riders[1]], axis=dim)
        got_up = lax.ppermute(send_up, axis, up)
        got_down = lax.ppermute(send_down, axis, down)
        if hop == 1 and riders is not None:
            width_up, width_down = length - start, stop
            carried = (
                lax.slice_in_dim(got_up, width_up, got_up.shape[dim], axis=dim),
                lax.slice_in_dim(got_down, width_down, got_down.shape[dim], axis=dim),
            )
            got_up = lax.slice_in_dim(got_up, 0, width_up, axis=dim)
            got_down = lax.slice_in_dim(got_down, 0, width_down, axis=dim)
        if (hop - 1) * length < before_width:
            pieces_before.insert(0, got_up)
        if (hop - 1) * length < after_width:
            pieces_after.append(got_down)
        hop += 1
    joined = jnp.concatenate(pieces_before + [shard] + pieces_after, axis=dim)
    return joined if riders is None else (joined, carried)


def band(kernel, n_in, n_out, sign, shift):
    offset = sign * (
        lax.broadcasted_iota(jnp.int32, (n_in, n_out), 0)
        - lax.broadcasted_iota(jnp.int32, (n_in, n_out), 1)
    ) + shift
    taps = lax.broadcasted_iota(jnp.int32, (1, 1, kernel.shape[0]), 2)
    picked = jnp.where(offset[:, :, None] == taps, kernel[None, None, :], 0.0)
    return jnp.sum(picked, axis=2)


def band_square(kernel, n, shift):
    block = 128
    taps = kernel.shape[0]
    if n % block or n == block or max(shift, taps - 1 - shift) >= block:
        return band(kernel, n, n, 1, shift)
    count = n // block
    parts = {
        d: band(kernel, block, block, 1, shift + d * block) for d in (-1, 0, 1)
    }
    zero = jnp.zeros((block, block), jnp.float32)
    rows = [
        jnp.concatenate([parts.get(i - j, zero) for j in range(count)], axis=1)
        for i in range(count)
    ]
    return jnp.concatenate(rows, axis=0)


def pyramid_matrix(row_count, col_count, anchor):
    offset_index = (
        lax.broadcasted_iota(jnp.int32, (row_count, col_count), 0)
        - 2 * lax.broadcasted_iota(jnp.int32, (row_count, col_count), 1)
        + anchor
    )
    outer = (offset_index == 0) | (offset_index == 3)
    middle = (offset_index == 1) | (offset_index == 2)
    return jnp.where(
        outer, jnp.float32(0.125), jnp.where(middle, jnp.float32(0.375), jnp.float32(0.0))
    )


def along_columns(volume, matrix, transpose=False):
    contract = 1 if transpose else 0
    return lax.dot_general(
        volume, matrix, (((2,), (contract,)), ((), ())), precision=PRECISE
    )


def along_rows(volume, matrix):
    planes = volume.shape[0]
    left = jnp.broadcast_to(matrix.T[None], (planes,) + matrix.T.shape)
    return lax.dot_general(
        left, volume, (((2,), (1,)), ((0,), (0,))), precision=PRECISE
    )


def along_planes(volume, matrix):
    return lax.dot_general(
        matrix.T, volume, (((1,), (0,)), ((), ())), precision=PRECISE
    )


def shards(estimate, observed, kernel_rows, kernel_columns, kernel_planes):
    plane_count, row_count, col_count = estimate.shape
    taps = kernel_rows.shape[0]
    reach = (taps - 1) // 2

    rows_ext = row_count + 2 * reach
    planes_ext = plane_count + 2 * reach
    bands = [
        band_square(kernel_columns, col_count, reach),
        band(kernel_rows, rows_ext, row_count, 1, 0),
        band(kernel_planes, planes_ext, plane_count, 1, 0),
        band(kernel_planes, planes_ext, plane_count, -1, 2 * reach),
        band(kernel_rows, rows_ext + 2, row_count + 2, -1, 2 * reach),
        pyramid_matrix(col_count, col_count // 2, 1),
        pyramid_matrix(row_count + 2, row_count // 2, 0),
    ]
    bands = [lax.optimization_barrier(matrix) for matrix in bands]
    col_band, row_fwd, plane_fwd, plane_back, row_back, pyr_cols, pyr_rows = bands

    filtered = along_columns(estimate, col_band)
    chunk = col_count // CHUNKS
    planes = plane_count
    last_row = lax.slice_in_dim(estimate, row_count - 1, row_count, axis=1)
    first_row = lax.slice_in_dim(estimate, 0, 1, axis=1)
    fold = (planes, CHUNKS, chunk)
    riders = (last_row.reshape(fold), first_row.reshape(fold))
    spreads = []
    for index in range(CHUNKS):
        part = lax.slice_in_dim(filtered, index * chunk, (index + 1) * chunk, axis=2)
        seen = lax.slice_in_dim(observed, index * chunk, (index + 1) * chunk, axis=2)
        z_first = index % 2 == 1
        blurred = part
        for along_z in ((True, False) if z_first else (False, True)):
            if along_z:
                blurred = along_planes(halo(blurred, "slab", 0, reach, reach), plane_fwd)
            elif index == 1:
                blurred, carried = halo(blurred, "tile", 1, reach, reach, riders)
                blurred = along_rows(blurred, row_fwd)
            else:
                blurred = along_rows(halo(blurred, "tile", 1, reach, reach), row_fwd)
        quotient = seen / blurred
        spread = quotient
        for along_z in ((True, False) if z_first else (False, True)):
            if along_z:
                spread = along_planes(halo(spread, "slab", 0, reach, reach), plane_back)
            else:
                spread = along_rows(halo(spread, "tile", 1, reach + 1, reach + 1), row_back)
        cols_of = lax.slice_in_dim(col_band, index * chunk, (index + 1) * chunk, axis=1)
        share = along_columns(spread, cols_of, transpose=True)
        spreads.append(share)
    correction = spreads[0]
    for share in spreads[1:]:
        correction = correction + share
    unfold = (planes, 1, col_count)
    edge_rows = jnp.concatenate(
        [carried[0].reshape(unfold), estimate, carried[1].reshape(unfold)], axis=1
    )
    new_ext = edge_rows * correction
    new_estimate = estimate * lax.slice_in_dim(correction, 1, row_count + 1, axis=1)

    halved = along_columns(new_ext, pyr_cols)
    pyramid_level = along_rows(halved, pyr_rows)
    return (new_estimate, pyramid_level)


def solution(mesh):
    in_specs = (P("slab", "tile", None), P("slab", "tile", None), P(), P(), P())
    out_specs = (P("slab", "tile", None), P("slab", "tile", None))
    return jax.shard_map(shards, mesh=mesh, in_specs=in_specs, out_specs=out_specs, check_vma=False)
```
